128 devices in a mesh: dom: 16 (over z, y), grp: 8 (over x, core).
Axes of the slice: x: 4, y: 4, z: 4, core: 2. Of those that a mesh axis runs over, the one named last changes fastest.
Arguments:
- residual_in: bfloat16 [1024, 32, 625], P(('dom', 'grp')), may hold values from -6 to 6
- block_inverse: bfloat16 [1024, 625, 625], P(('dom', 'grp')), may hold values from -0.25 to 0.25
- coupling: bfloat16 [2048, 625, 625], P(('dom', 'grp')), may hold values from -0.25 to 0.25
- tile_region: int32 [2048, 1], P(('dom', 'grp')), may hold values from 0 to 15; in each aligned block of 16 rows (0 to 15, 16 to 31, ...) at most 2 rows name the same one
- tile_source: int32 [2048], P(('dom', 'grp')), may hold values from 0 to 7
- tile_target: int32 [2048], P(('dom', 'grp')), may hold values from 0 to 7
- interface_basis: bfloat16 [1024, 625, 64], P(('dom', 'grp')), may hold values from -0.25 to 0.25
- reduced_inverse: float32 [16, 64, 64], P('dom'), may hold values from -0.75 to 0.75
Outputs:
- preconditioned: float32 [1024, 32, 625], P(('dom', 'grp'))
The draws below stay inside these ranges and needn't reach their ends.
Inputs may be any that keep to these rules, and one draw needn't show every extreme that they name: `tile_region`: among the 16 tiles of one device, at most 2 name the same region; in every draw some device names some region exactly 2 times.
All inputs are finite; a program needn't handle non-finite values.
Results may differ from the reference program's by a relative error of at most 0.013.
Values may be sent and summed in bfloat16 or wider, within the bound.
No kernel may reach another device: no remote copies, remote signals or barrier semaphores. Data moves between devices by JAX's collectives and lax.ppermute only.
A program may use at most 256 MiB of HBM per device.

```python
import math
import jax
import jax.numpy as jnp
import numpy as np
from jax import lax

B = 625
K = 32
M = 64
CAP = 2
EL = 8
TL = 16
E_TOT = 1024
TILES = 2048
N_DOM = 16
N_GRP = 8


def plant(result, own_key, low, high):
    shape = result.shape
    index_at = [jax.random.randint(jax.random.fold_in(own_key, axis), (), 0, shape[axis]) for axis in range(len(shape))]
    result = result.at[tuple(index_at)].set(low)
    longest = shape.index(max(shape))
    index_at[longest] = (index_at[longest] + 1) % shape[longest]
    return result.at[tuple(index_at)].set(high)


def block_levels(stream_key, extent, pieces, smallest, top_value):
    level, own = 1.0, jax.random.fold_in(stream_key, 6)
    for position, blocks in pieces:
        draws = jnp.exp(jax.random.uniform(jax.random.fold_in(own, position), (blocks,), jnp.float32, smallest / len(pieces), top_value / len(pieces)))
        level = level * jnp.repeat(draws, extent[position] // blocks).reshape([-1 if axis == position else 1 for axis in range(len(extent))])
    return level


def assign_block(rng, own, number, rows, number_of, top, most, skew):
    order = jax.random.permutation(rng, number_of)
    crowded, usual = shares(number_of, rows * top, most, skew, True), shares(number_of, rows * top, most, skew, False)
    places = jnp.arange(number_of)

    def named(tallies, rotation):
        used = int((tallies > 0).sum())
        fixed = max(1, used // 4)
        moved = fixed + (places - fixed + rotation * (used - fixed)) % max(1, number_of - fixed)
        return jnp.zeros((number_of,), jnp.int32).at[order[jnp.where(places < fixed, places, moved)]].set(jnp.asarray(tallies, jnp.int32))

    tallies = jnp.where(number % 4 == 0, named(crowded, number // 4), named(usual, number - number // 4 - 1))
    mixed = jax.random.permutation(jax.random.fold_in(own, 3), number_of)
    source_of, taker = mixed[0:number_of // 2 * 2:2], mixed[1:number_of // 2 * 2:2]
    margin = jnp.minimum(tallies[source_of] - 1, most - tallies[taker]) // 2
    margin = jnp.where((source_of == order[0]) | (taker == order[0]) | (tallies[taker] == 0), 0, jnp.maximum(margin, 0))
    moved = jax.random.randint(jax.random.fold_in(own, 4), (number_of // 2,), 0, 1 << 20) % (margin + 1)
    tallies = tallies.at[source_of].add(-moved).at[taker].add(moved)
    labels = jnp.searchsorted(jnp.cumsum(tallies), jnp.arange(rows * top), side="right").astype(jnp.int32)
    grid = labels.reshape(top, rows).T
    grid = grid[jax.random.permutation(jax.random.fold_in(own, 1), rows)]
    rotation = jax.random.randint(jax.random.fold_in(own, 2), (rows, 1), 0, top)
    return jnp.take_along_axis(grid, (jnp.arange(top)[None, :] + rotation) % top, axis=1)


def shares(number_of, total, bound, skew, full):
    loads = [(1 << 20) // math.isqrt(standing ** skew) + 1 for standing in range(1, number_of + 1)]
    largest = bound if full else min(bound, max(-(-total // number_of), total * loads[0] // sum(loads)))
    least = 1 if total - largest >= number_of - 1 else 0
    given, surplus = [largest] + [least] * (number_of - 1), total - largest - least * (number_of - 1)
    while surplus > 0:
        movable = [i for i in range(1, number_of) if given[i] < largest] or [i for i in range(1, number_of) if given[i] < bound]
        pool, left = sum([loads[i] for i in movable]), surplus
        for i in movable:
            extra = min(bound - given[i], max(1, left * loads[i] // pool), surplus)
            given[i] = given[i] + extra
            surplus = surplus - extra
    return np.array(given)


def scatter_about(own_key, extent, scale, reach, shards=(), held_as=jnp.bfloat16):
    array = jax.random.normal(own_key, extent, jnp.float32) * scale
    if len(shards) > 0:
        array = block_levels(own_key, extent, shards, -0.22, 0.18) * array
    return jnp.clip(array, min=-reach, max=reach).astype(held_as)


def setup_inputs(seed: int = 0) -> dict:
    key_of = jax.random.split(jax.random.key(seed), 9)
    residual_in = scatter_about(key_of[0], (E_TOT, K, B), 1.0, 6.0, ((0, 128),))
    block_inverse = scatter_about(key_of[1], (E_TOT, B, B), B ** -0.5, 0.25, ((0, 128),))
    coupling = scatter_about(key_of[2], (TILES, B, B), B ** -0.5, 0.25, ((0, 128),))
    tile_region_keys = jax.random.split(jax.random.fold_in(key_of[3], 1), TILES // TL)
    tile_region_turns = jax.random.permutation(jax.random.fold_in(key_of[3], 3), TILES // TL)
    tile_region = jax.vmap(lambda own, number: assign_block(jax.random.fold_in(key_of[3], 2), own, number, TL, N_DOM, 1, CAP, 2))(tile_region_keys, tile_region_turns).reshape((TILES, 1))
    tile_source = plant(jax.random.randint(key_of[4], (TILES,), 0, EL), jax.random.fold_in(key_of[4], 1), 0, EL - 1).astype(jnp.int32)
    tile_target = plant(jax.random.randint(key_of[5], (TILES,), 0, EL), jax.random.fold_in(key_of[5], 1), 0, EL - 1).astype(jnp.int32)
    interface_basis = scatter_about(key_of[6], (E_TOT, B, M), B ** -0.5, 0.25, ((0, 128),))
    reduced_inverse = scatter_about(key_of[7], (N_DOM, M, M), M ** -0.5, 0.75, ((0, 16),), jnp.float32)
    return dict(residual_in=residual_in, block_inverse=block_inverse, coupling=coupling, tile_region=tile_region, tile_source=tile_source, tile_target=tile_target, interface_basis=interface_basis, reduced_inverse=reduced_inverse)


def apply_blocks(values, blocks):
    return lax.map(lambda pair: jnp.dot(pair[0], pair[1], preferred_element_type=jnp.float32), (values, blocks))


def reference(residual_in, block_inverse, coupling, tile_region, tile_source, tile_target, interface_basis, reduced_inverse):
    e_total = residual_in.shape[0]
    t_total = coupling.shape[0]
    initial = apply_blocks(residual_in, block_inverse).astype(jnp.bfloat16)
    owner = (jnp.arange(t_total, dtype=jnp.int32) // TL).astype(jnp.int32)
    source_global = owner * EL + tile_source
    target_dev = tile_region[:, 0] * N_GRP + owner % N_GRP
    target_global = (target_dev * EL + tile_target).astype(jnp.int32)
    gathered = initial[source_global]
    products = apply_blocks(gathered, coupling)
    coupled = jax.ops.segment_sum(products, target_global, num_segments=e_total)
    corrected_in = (residual_in.astype(jnp.float32) - coupled).astype(jnp.bfloat16)
    second = apply_blocks(corrected_in, block_inverse)
    second_b = second.astype(jnp.bfloat16)
    per_element = apply_blocks(second_b, interface_basis)
    reduced = per_element.reshape(N_DOM, N_GRP * EL, K, M).sum(axis=1)
    solved = jnp.einsum("rkm,rmn->rkn", reduced, reduced_inverse, precision=lax.Precision.HIGHEST).astype(jnp.bfloat16)
    spread = jnp.repeat(solved, N_GRP * EL, axis=0)
    correction = lax.map(lambda pair: jnp.dot(pair[0], pair[1].T, preferred_element_type=jnp.float32), (spread, interface_basis))
    return second + correction
```

```python
import jax
import jax.numpy as jnp
from jax import lax
from jax.sharding import PartitionSpec as P

CAP = 2
LANE = 128


def group_sum(value, axis):
    size = lax.axis_size(axis)
    if size & (size - 1):
        return lax.psum(value, axis)
    bit = 1
    while bit < size:
        pairs = [(i, i ^ bit) for i in range(size)]
        value = value + lax.ppermute(value, axis, pairs)
        bit *= 2
    return value


def shards(
    residual_in,
    block_inverse,
    coupling,
    tile_region,
    tile_source,
    tile_target,
    interface_basis,
    reduced_inverse,
):
    regions = lax.axis_size("dom")
    slots = regions * CAP
    elements = residual_in.shape[0]
    vectors = residual_in.shape[1]
    width = residual_in.shape[2]
    tiles = coupling.shape[0]
    padded = -(-(width + 1) // LANE) * LANE
    initial = jnp.einsum(
        "ekb,ebc->ekc", residual_in, block_inverse, preferred_element_type=jnp.float32
    ).astype(jnp.bfloat16)
    destination = tile_region[:, 0]
    order = jnp.arange(tiles, dtype=jnp.int32)
    same = destination[:, None] == destination[None, :]
    tile_rank = jnp.sum(same & (order[None, :] < order[:, None]), axis=1).astype(jnp.int32)
    slot_index = destination * CAP + tile_rank
    slot_ids = jnp.arange(slots, dtype=jnp.int32)
    hit = slot_index[None, :] == slot_ids[:, None]
    slot_tile = jnp.where(
        jnp.any(hit, axis=1), jnp.sum(jnp.where(hit, order[None, :], 0), axis=1), tiles
    ).astype(jnp.int32)
    sources = initial[tile_source]
    local_products = jnp.einsum(
        "tkb,tbc->tkc", sources, coupling, preferred_element_type=jnp.float32
    ).astype(jnp.bfloat16)
    marks = jnp.concatenate([tile_target, jnp.full((1,), -1, jnp.int32)]).astype(jnp.bfloat16)
    column = lax.broadcasted_iota(jnp.int32, (tiles + 1, vectors, padded - width), 2)
    row = lax.broadcasted_iota(jnp.int32, (tiles + 1, vectors, padded - width), 1)
    tail = jnp.where((column == 0) & (row == 0), marks[:, None, None], jnp.bfloat16(0))
    body = jnp.concatenate(
        [local_products, jnp.zeros((1, vectors, width), jnp.bfloat16)], axis=0
    )
    extended = jnp.concatenate([body, tail], axis=2)
    product_buffer = extended[slot_tile]
    received = lax.all_to_all(
        product_buffer.reshape(regions, CAP, vectors, padded),
        "dom",
        split_axis=0,
        concat_axis=0,
        tiled=True,
    ).reshape(slots, vectors, padded)
    targets = received[:, 0, width].astype(jnp.int32)
    products = received[:, :, :width]
    selector = (targets[None, :] == jnp.arange(elements, dtype=jnp.int32)[:, None]).astype(
        jnp.bfloat16
    )
    coupled = jnp.einsum(
        "es,skc->ekc", selector, products, preferred_element_type=jnp.float32
    )
    corrected_in = (residual_in.astype(jnp.float32) - coupled).astype(jnp.bfloat16)
    second = jnp.einsum(
        "ekb,ebc->ekc", corrected_in, block_inverse, preferred_element_type=jnp.float32
    )
    second_b = second.astype(jnp.bfloat16)
    partial_reduced = jnp.einsum(
        "ekb,ebm->km", second_b, interface_basis, preferred_element_type=jnp.float32
    )
    reduced = group_sum(partial_reduced, "grp")
    solved = jnp.dot(
        reduced,
        reduced_inverse[0],
        precision=lax.Precision.HIGHEST,
        preferred_element_type=jnp.float32,
    ).astype(jnp.bfloat16)
    correction = jnp.einsum(
        "km,ebm->ekb", solved, interface_basis, preferred_element_type=jnp.float32
    )
    return second + correction


def solution(mesh):
    return jax.shard_map(
        shards,
        mesh=mesh,
        in_specs=(
            P(("dom", "grp"), None, None),
            P(("dom", "grp"), None, None),
            P(("dom", "grp"), None, None),
            P(("dom", "grp"), None),
            P(("dom", "grp")),
            P(("dom", "grp")),
            P(("dom", "grp"), None, None),
            P("dom", None, None),
        ),
        out_specs=P(("dom", "grp"), None, None),
        check_vma=False,
    )
```

```python
import jax
import jax.numpy as jnp
from jax import lax
from jax.sharding import PartitionSpec as P

CAP = 2
LANE = 128


def group_sum(value, axis):
    size = lax.axis_size(axis)
    if size & (size - 1):
        return lax.psum(value, axis)
    bit = 1
    while bit < size:
        pairs = [(i, i ^ bit) for i in range(size)]
        value = value + lax.ppermute(value, axis, pairs)
        bit *= 2
    return value


def shards(
    residual_in,
    block_inverse,
    coupling,
    tile_region,
    tile_source,
    tile_target,
    interface_basis,
    reduced_inverse,
):
    regions = lax.axis_size("dom")
    slots = regions * CAP
    elements = residual_in.shape[0]
    vectors = residual_in.shape[1]
    width = residual_in.shape[2]
    tiles = coupling.shape[0]
    padded = -(-(width + 1) // LANE) * LANE
    initial = jnp.einsum(
        "ekb,ebc->ekc", residual_in, block_inverse, preferred_element_type=jnp.float32
    ).astype(jnp.bfloat16)
    destination = tile_region[:, 0]
    order = jnp.arange(tiles, dtype=jnp.int32)
    same = destination[:, None] == destination[None, :]
    tile_rank = jnp.sum(same & (order[None, :] < order[:, None]), axis=1).astype(jnp.int32)
    slot_index = destination * CAP + tile_rank
    slot_ids = jnp.arange(slots, dtype=jnp.int32)
    hit = slot_index[None, :] == slot_ids[:, None]
    slot_tile = jnp.where(
        jnp.any(hit, axis=1), jnp.sum(jnp.where(hit, order[None, :], 0), axis=1), tiles
    ).astype(jnp.int32)
    sources = initial[tile_source]
    local_products = jnp.einsum(
        "tkb,tbc->tkc", sources, coupling, preferred_element_type=jnp.float32
    ).astype(jnp.bfloat16)
    marks = jnp.concatenate([tile_target, jnp.full((1,), -1, jnp.int32)]).astype(jnp.bfloat16)
    column = lax.broadcasted_iota(jnp.int32, (tiles + 1, vectors, padded - width), 2)
    row = lax.broadcasted_iota(jnp.int32, (tiles + 1, vectors, padded - width), 1)
    tail = jnp.where((column == 0) & (row == 0), marks[:, None, None], jnp.bfloat16(0))
    body = jnp.concatenate(
        [local_products, jnp.zeros((1, vectors, width), jnp.bfloat16)], axis=0
    )
    extended = jnp.concatenate([body, tail], axis=2)
    product_buffer = extended[slot_tile]
    received = lax.all_to_all(
        product_buffer.reshape(regions, CAP, vectors, padded),
        "dom",
        split_axis=0,
        concat_axis=0,
        tiled=True,
    ).reshape(slots, vectors, padded)
    targets = received[:, 0, width].astype(jnp.int32)
    products = received[:, :, :width]
    selector = (targets[None, :] == jnp.arange(elements, dtype=jnp.int32)[:, None]).astype(
        jnp.bfloat16
    )
    coupled = jnp.einsum(
        "es,skc->ekc", selector, products, preferred_element_type=jnp.float32
    )
    corrected_in = (residual_in.astype(jnp.float32) - coupled).astype(jnp.bfloat16)
    projected = jnp.einsum(
        "ebc,ecm->ebm", block_inverse, interface_basis, preferred_element_type=jnp.float32
    )
    projected_hi = projected.astype(jnp.bfloat16)
    projected_lo = (projected - projected_hi.astype(jnp.float32)).astype(jnp.bfloat16)
    partial_reduced = jnp.einsum(
        "ekb,ebm->km", corrected_in, projected_hi, preferred_element_type=jnp.float32
    ) + jnp.einsum(
        "ekb,ebm->km", corrected_in, projected_lo, preferred_element_type=jnp.float32
    )
    reduced = group_sum(partial_reduced, "grp")
    second = jnp.einsum(
        "ekb,ebc->ekc", corrected_in, block_inverse, preferred_element_type=jnp.float32
    )
    solved = jnp.dot(
        reduced,
        reduced_inverse[0],
        precision=lax.Precision.HIGHEST,
        preferred_element_type=jnp.float32,
    ).astype(jnp.bfloat16)
    correction = jnp.einsum(
        "km,ebm->ekb", solved, interface_basis, preferred_element_type=jnp.float32
    )
    return second + correction


def solution(mesh):
    return jax.shard_map(
        shards,
        mesh=mesh,
        in_specs=(
            P(("dom", "grp"), None, None),
            P(("dom", "grp"), None, None),
            P(("dom", "grp"), None, None),
            P(("dom", "grp"), None),
            P(("dom", "grp")),
            P(("dom", "grp")),
            P(("dom", "grp"), None, None),
            P("dom", None, None),
        ),
        out_specs=P(("dom", "grp"), None, None),
        check_vma=False,
    )
```

```python
import jax
import jax.numpy as jnp
from jax import lax
from jax.sharding import PartitionSpec as P

CAP = 2
LANE = 128


def group_sum(value, axis):
    size = lax.axis_size(axis)
    if size & (size - 1):
        return lax.psum(value, axis)
    bit = 1
    while bit < size:
        pairs = [(i, i ^ bit) for i in range(size)]
        value = value + lax.ppermute(value, axis, pairs)
        bit *= 2
    return value


def shards(
    residual_in,
    block_inverse,
    coupling,
    tile_region,
    tile_source,
    tile_target,
    interface_basis,
    reduced_inverse,
):
    regions = lax.axis_size("dom")
    slots = regions * CAP
    elements = residual_in.shape[0]
    vectors = residual_in.shape[1]
    width = residual_in.shape[2]
    tiles = coupling.shape[0]
    padded = -(-(width + 1) // LANE) * LANE
    initial = jnp.einsum(
        "ekb,ebc->ekc", residual_in, block_inverse, preferred_element_type=jnp.float32
    ).astype(jnp.bfloat16)
    info = lax.optimization_barrier(
        jnp.concatenate([tile_region[:, 0], tile_source, tile_target])
    )
    destination = info[:tiles]
    tile_source = info[tiles : 2 * tiles]
    tile_target = info[2 * tiles :]
    order = jnp.arange(tiles, dtype=jnp.int32)
    same = destination[:, None] == destination[None, :]
    tile_rank = jnp.sum(same & (order[None, :] < order[:, None]), axis=1).astype(jnp.int32)
    slot_index = destination * CAP + tile_rank
    slot_ids = jnp.arange(slots, dtype=jnp.int32)
    hit = slot_index[None, :] == slot_ids[:, None]
    slot_tile = jnp.where(
        jnp.any(hit, axis=1), jnp.sum(jnp.where(hit, order[None, :], 0), axis=1), tiles
    ).astype(jnp.int32)
    sources = initial[tile_source]
    local_products = jnp.einsum(
        "tkb,tbc->tkc", sources, coupling, preferred_element_type=jnp.float32
    ).astype(jnp.bfloat16)
    marks = jnp.concatenate([tile_target, jnp.full((1,), -1, jnp.int32)]).astype(jnp.bfloat16)
    column = lax.broadcasted_iota(jnp.int32, (tiles + 1, vectors, padded - width), 2)
    row = lax.broadcasted_iota(jnp.int32, (tiles + 1, vectors, padded - width), 1)
    tail = jnp.where((column == 0) & (row == 0), marks[:, None, None], jnp.bfloat16(0))
    body = jnp.concatenate(
        [local_products, jnp.zeros((1, vectors, width), jnp.bfloat16)], axis=0
    )
    extended = jnp.concatenate([body, tail], axis=2)
    product_buffer = extended[slot_tile]
    received = lax.all_to_all(
        product_buffer.reshape(regions, CAP, vectors, padded),
        "dom",
        split_axis=0,
        concat_axis=0,
        tiled=True,
    ).reshape(slots, vectors, padded)
    targets = received[:, 0, width].astype(jnp.int32)
    products = received[:, :, :width]
    selector = (targets[None, :] == jnp.arange(elements, dtype=jnp.int32)[:, None]).astype(
        jnp.bfloat16
    )
    coupled = jnp.einsum(
        "es,skc->ekc", selector, products, preferred_element_type=jnp.float32
    )
    corrected_in = (residual_in.astype(jnp.float32) - coupled).astype(jnp.bfloat16)
    projected = jnp.einsum(
        "ebc,ecm->ebm", block_inverse, interface_basis, preferred_element_type=jnp.float32
    )
    projected_hi = projected.astype(jnp.bfloat16)
    projected_lo = (projected - projected_hi.astype(jnp.float32)).astype(jnp.bfloat16)
    partial_reduced = jnp.einsum(
        "ekb,ebm->km", corrected_in, projected_hi, preferred_element_type=jnp.float32
    ) + jnp.einsum(
        "ekb,ebm->km", corrected_in, projected_lo, preferred_element_type=jnp.float32
    )
    reduced = group_sum(partial_reduced, "grp")
    half = elements // 2
    second = jnp.concatenate(
        [
            jnp.einsum(
                "ekb,ebc->ekc",
                corrected_in[:half],
                block_inverse[:half],
                preferred_element_type=jnp.float32,
            ),
            jnp.einsum(
                "ekb,ebc->ekc",
                corrected_in[half:],
                block_inverse[half:],
                preferred_element_type=jnp.float32,
            ),
        ],
        axis=0,
    )
    solved = jnp.dot(
        reduced,
        reduced_inverse[0],
        precision=lax.Precision.HIGHEST,
        preferred_element_type=jnp.float32,
    ).astype(jnp.bfloat16)
    correction = jnp.einsum(
        "km,ebm->ekb", solved, interface_basis, preferred_element_type=jnp.float32
    )
    return second + correction


def solution(mesh):
    return jax.shard_map(
        shards,
        mesh=mesh,
        in_specs=(
            P(("dom", "grp"), None, None),
            P(("dom", "grp"), None, None),
            P(("dom", "grp"), None, None),
            P(("dom", "grp"), None),
            P(("dom", "grp")),
            P(("dom", "grp")),
            P(("dom", "grp"), None, None),
            P("dom", None, None),
        ),
        out_specs=P(("dom", "grp"), None, None),
        check_vma=False,
    )
```

```python
import jax
import jax.numpy as jnp
from jax import lax
from jax.sharding import PartitionSpec as P

CAP = 2
LANE = 128


def group_sum(value, axis):
    size = lax.axis_size(axis)
    if size & (size - 1):
        return lax.psum(value, axis)
    bit = 1
    while bit < size:
        pairs = [(i, i ^ bit) for i in range(size)]
        value = value + lax.ppermute(value, axis, pairs)
        bit *= 2
    return value


def shards(
    residual_in,
    block_inverse,
    coupling,
    tile_region,
    tile_source,
    tile_target,
    interface_basis,
    reduced_inverse,
):
    regions = lax.axis_size("dom")
    slots = regions * CAP
    elements = residual_in.shape[0]
    vectors = residual_in.shape[1]
    width = residual_in.shape[2]
    tiles = coupling.shape[0]
    padded = -(-(width + 1) // LANE) * LANE
    initial = jnp.einsum(
        "ekb,ebc->ekc", residual_in, block_inverse, preferred_element_type=jnp.float32
    ).astype(jnp.bfloat16)
    info = lax.optimization_barrier(
        jnp.concatenate([tile_region[:, 0], tile_source, tile_target])
    )
    destination = info[:tiles]
    tile_source = info[tiles : 2 * tiles]
    tile_target = info[2 * tiles :]
    order = jnp.arange(tiles, dtype=jnp.int32)
    same = destination[:, None] == destination[None, :]
    tile_rank = jnp.sum(same & (order[None, :] < order[:, None]), axis=1).astype(jnp.int32)
    slot_index = destination * CAP + tile_rank
    slot_ids = jnp.arange(slots, dtype=jnp.int32)
    hit = slot_index[None, :] == slot_ids[:, None]
    slot_tile = jnp.where(
        jnp.any(hit, axis=1), jnp.sum(jnp.where(hit, order[None, :], 0), axis=1), tiles
    ).astype(jnp.int32)
    sources = initial[tile_source]
    local_products = jnp.einsum(
        "tkb,tbc->tkc", sources, coupling, preferred_element_type=jnp.float32
    ).astype(jnp.bfloat16)
    marks = jnp.concatenate([tile_target, jnp.full((1,), -1, jnp.int32)]).astype(jnp.bfloat16)
    column = lax.broadcasted_iota(jnp.int32, (tiles + 1, vectors, padded - width), 2)
    row = lax.broadcasted_iota(jnp.int32, (tiles + 1, vectors, padded - width), 1)
    tail = jnp.where((column == 0) & (row == 0), marks[:, None, None], jnp.bfloat16(0))
    body = jnp.concatenate(
        [local_products, jnp.zeros((1, vectors, width), jnp.bfloat16)], axis=0
    )
    extended = jnp.concatenate([body, tail], axis=2)
    product_buffer = extended[slot_tile]
    received = lax.all_to_all(
        product_buffer.reshape(regions, CAP, vectors, padded),
        "dom",
        split_axis=0,
        concat_axis=0,
        tiled=True,
    ).reshape(slots, vectors, padded)
    targets = received[:, 0, width].astype(jnp.int32)
    products = received[:, :, :width]
    selector = (targets[None, :] == jnp.arange(elements, dtype=jnp.int32)[:, None]).astype(
        jnp.bfloat16
    )
    coupled = jnp.einsum(
        "es,skc->ekc", selector, products, preferred_element_type=jnp.float32
    )
    corrected_in = (residual_in.astype(jnp.float32) - coupled).astype(jnp.bfloat16)
    projected = jnp.einsum(
        "ebc,ecm->ebm", block_inverse, interface_basis, preferred_element_type=jnp.float32
    )
    partial_reduced = jnp.einsum(
        "ekb,ebm->km",
        corrected_in,
        projected.astype(jnp.bfloat16),
        preferred_element_type=jnp.float32,
    )
    reduced = group_sum(partial_reduced, "grp")
    half = elements // 2
    second = jnp.concatenate(
        [
            jnp.einsum(
                "ekb,ebc->ekc",
                corrected_in[:half],
                block_inverse[:half],
                preferred_element_type=jnp.float32,
            ),
            jnp.einsum(
                "ekb,ebc->ekc",
                corrected_in[half:],
                block_inverse[half:],
                preferred_element_type=jnp.float32,
            ),
        ],
        axis=0,
    )
    solved = jnp.dot(
        reduced,
        reduced_inverse[0],
        precision=lax.Precision.HIGHEST,
        preferred_element_type=jnp.float32,
    ).astype(jnp.bfloat16)
    correction = jnp.einsum(
        "km,ebm->ekb", solved, interface_basis, preferred_element_type=jnp.float32
    )
    return second + correction


def solution(mesh):
    return jax.shard_map(
        shards,
        mesh=mesh,
        in_specs=(
            P(("dom", "grp"), None, None),
            P(("dom", "grp"), None, None),
            P(("dom", "grp"), None, None),
            P(("dom", "grp"), None),
            P(("dom", "grp")),
            P(("dom", "grp")),
            P(("dom", "grp"), None, None),
            P("dom", None, None),
        ),
        out_specs=P(("dom", "grp"), None, None),
        check_vma=False,
    )
```

```python
import jax
import jax.numpy as jnp
from jax import lax
from jax.sharding import PartitionSpec as P

CAP = 2
LANE = 128


def group_sum(value, axis):
    size = lax.axis_size(axis)
    if size & (size - 1):
        return lax.psum(value, axis)
    bit = 1
    while bit < size:
        pairs = [(i, i ^ bit) for i in range(size)]
        value = value + lax.ppermute(value, axis, pairs)
        bit *= 2
    return value


def shards(
    residual_in,
    block_inverse,
    coupling,
    tile_region,
    tile_source,
    tile_target,
    interface_basis,
    reduced_inverse,
):
    regions = lax.axis_size("dom")
    slots = regions * CAP
    elements = residual_in.shape[0]
    vectors = residual_in.shape[1]
    width = residual_in.shape[2]
    tiles = coupling.shape[0]
    padded = -(-(width + 1) // LANE) * LANE
    initial = jnp.einsum(
        "ekb,ebc->ekc", residual_in, block_inverse, preferred_element_type=jnp.float32
    ).astype(jnp.bfloat16)
    info = lax.optimization_barrier(
        jnp.concatenate([tile_region[:, 0], tile_source, tile_target])
    )
    destination = info[:tiles]
    tile_source = info[tiles : 2 * tiles]
    tile_target = info[2 * tiles :]
    order = jnp.arange(tiles, dtype=jnp.int32)
    same = destination[:, None] == destination[None, :]
    tile_rank = jnp.sum(same & (order[None, :] < order[:, None]), axis=1).astype(jnp.int32)
    slot_index = destination * CAP + tile_rank
    slot_ids = jnp.arange(slots, dtype=jnp.int32)
    hit = slot_index[None, :] == slot_ids[:, None]
    slot_tile = jnp.where(
        jnp.any(hit, axis=1), jnp.sum(jnp.where(hit, order[None, :], 0), axis=1), tiles
    ).astype(jnp.int32)
    sources = initial[tile_source]
    local_products = jnp.einsum(
        "tkb,tbc->tkc", sources, coupling, preferred_element_type=jnp.float32
    ).astype(jnp.bfloat16)
    marks = jnp.concatenate([tile_target, jnp.full((1,), -1, jnp.int32)]).astype(jnp.bfloat16)
    column = lax.broadcasted_iota(jnp.int32, (tiles + 1, vectors, padded - width), 2)
    row = lax.broadcasted_iota(jnp.int32, (tiles + 1, vectors, padded - width), 1)
    tail = jnp.where((column == 0) & (row == 0), marks[:, None, None], jnp.bfloat16(0))
    body = jnp.concatenate(
        [local_products, jnp.zeros((1, vectors, width), jnp.bfloat16)], axis=0
    )
    extended = jnp.concatenate([body, tail], axis=2)
    product_buffer = extended[slot_tile]
    received = lax.all_to_all(
        product_buffer.reshape(regions, CAP, vectors, padded),
        "dom",
        split_axis=0,
        concat_axis=0,
        tiled=True,
    ).reshape(slots, vectors, padded)
    targets = received[:, 0, width].astype(jnp.int32)
    products = received[:, :, :width]
    selector = (targets[None, :] == jnp.arange(elements, dtype=jnp.int32)[:, None]).astype(
        jnp.bfloat16
    )
    coupled = jnp.einsum(
        "es,skc->ekc", selector, products, preferred_element_type=jnp.float32
    )
    corrected_in = (residual_in.astype(jnp.float32) - coupled).astype(jnp.bfloat16)
    projected = jnp.einsum(
        "ebc,ecm->ebm", block_inverse, interface_basis, preferred_element_type=jnp.float32
    )
    partial_reduced = jnp.einsum(
        "ekb,ebm->km",
        corrected_in,
        lax.optimization_barrier(projected.astype(jnp.bfloat16)),
        preferred_element_type=jnp.float32,
    )
    reduced = group_sum(partial_reduced, "grp")
    half = elements // 2
    second = jnp.concatenate(
        [
            jnp.einsum(
                "ekb,ebc->ekc",
                corrected_in[:half],
                block_inverse[:half],
                preferred_element_type=jnp.float32,
            ),
            jnp.einsum(
                "ekb,ebc->ekc",
                corrected_in[half:],
                block_inverse[half:],
                preferred_element_type=jnp.float32,
            ),
        ],
        axis=0,
    )
    solved = jnp.dot(
        reduced,
        reduced_inverse[0],
        precision=lax.Precision.HIGHEST,
        preferred_element_type=jnp.float32,
    ).astype(jnp.bfloat16)
    correction = jnp.einsum(
        "km,ebm->ekb", solved, interface_basis, preferred_element_type=jnp.float32
    )
    return second + correction


def solution(mesh):
    return jax.shard_map(
        shards,
        mesh=mesh,
        in_specs=(
            P(("dom", "grp"), None, None),
            P(("dom", "grp"), None, None),
            P(("dom", "grp"), None, None),
            P(("dom", "grp"), None),
            P(("dom", "grp")),
            P(("dom", "grp")),
            P(("dom", "grp"), None, None),
            P("dom", None, None),
        ),
        out_specs=P(("dom", "grp"), None, None),
        check_vma=False,
    )
```

```python
import jax
import jax.numpy as jnp
from jax import lax
from jax.sharding import PartitionSpec as P

CAP = 2
LANE = 128


def group_sum(value, axis):
    size = lax.axis_size(axis)
    if size & (size - 1):
        return lax.psum(value, axis)
    if size == 8:
        value = value + lax.ppermute(value, axis, [(i, i ^ 1) for i in range(size)])
        parts = [value] + [
            lax.ppermute(value, axis, [(i, (i + shift) % size) for i in range(size)])
            for shift in (2, 4, 6)
        ]
        return (parts[0] + parts[2]) + (parts[1] + parts[3])
    bit = 1
    while bit < size:
        pairs = [(i, i ^ bit) for i in range(size)]
        value = value + lax.ppermute(value, axis, pairs)
        bit *= 2
    return value


def shards(
    residual_in,
    block_inverse,
    coupling,
    tile_region,
    tile_source,
    tile_target,
    interface_basis,
    reduced_inverse,
):
    regions = lax.axis_size("dom")
    slots = regions * CAP
    elements = residual_in.shape[0]
    vectors = residual_in.shape[1]
    width = residual_in.shape[2]
    tiles = coupling.shape[0]
    padded = -(-(width + 1) // LANE) * LANE
    initial = jnp.einsum(
        "ekb,ebc->ekc", residual_in, block_inverse, preferred_element_type=jnp.float32
    ).astype(jnp.bfloat16)
    info = lax.optimization_barrier(
        jnp.concatenate([tile_region[:, 0], tile_source, tile_target])
    )
    destination = info[:tiles]
    tile_source = info[tiles : 2 * tiles]
    tile_target = info[2 * tiles :]
    order = jnp.arange(tiles, dtype=jnp.int32)
    same = destination[:, None] == destination[None, :]
    tile_rank = jnp.sum(same & (order[None, :] < order[:, None]), axis=1).astype(jnp.int32)
    slot_index = destination * CAP + tile_rank
    slot_ids = jnp.arange(slots, dtype=jnp.int32)
    hit = slot_index[None, :] == slot_ids[:, None]
    slot_tile = jnp.where(
        jnp.any(hit, axis=1), jnp.sum(jnp.where(hit, order[None, :], 0), axis=1), tiles
    ).astype(jnp.int32)
    sources = initial[tile_source]
    local_products = jnp.einsum(
        "tkb,tbc->tkc", sources, coupling, preferred_element_type=jnp.float32
    ).astype(jnp.bfloat16)
    marks = jnp.concatenate([tile_target, jnp.full((1,), -1, jnp.int32)]).astype(jnp.bfloat16)
    column = lax.broadcasted_iota(jnp.int32, (tiles + 1, vectors, padded - width), 2)
    row = lax.broadcasted_iota(jnp.int32, (tiles + 1, vectors, padded - width), 1)
    tail = jnp.where((column == 0) & (row == 0), marks[:, None, None], jnp.bfloat16(0))
    body = jnp.concatenate(
        [local_products, jnp.zeros((1, vectors, width), jnp.bfloat16)], axis=0
    )
    extended = jnp.concatenate([body, tail], axis=2)
    product_buffer = extended[slot_tile]
    received = lax.all_to_all(
        product_buffer.reshape(regions, CAP, vectors, padded),
        "dom",
        split_axis=0,
        concat_axis=0,
        tiled=True,
    ).reshape(slots, vectors, padded)
    targets = received[:, 0, width].astype(jnp.int32)
    products = received[:, :, :width]
    selector = (targets[None, :] == jnp.arange(elements, dtype=jnp.int32)[:, None]).astype(
        jnp.bfloat16
    )
    coupled = jnp.einsum(
        "es,skc->ekc", selector, products, preferred_element_type=jnp.float32
    )
    corrected_in = (residual_in.astype(jnp.float32) - coupled).astype(jnp.bfloat16)
    projected = jnp.einsum(
        "ebc,ecm->ebm", block_inverse, interface_basis, preferred_element_type=jnp.float32
    )
    partial_reduced = jnp.einsum(
        "ekb,ebm->km",
        corrected_in,
        lax.optimization_barrier(projected.astype(jnp.bfloat16)),
        preferred_element_type=jnp.float32,
    )
    reduced = group_sum(partial_reduced, "grp")
    half = elements // 2
    second = jnp.concatenate(
        [
            jnp.einsum(
                "ekb,ebc->ekc",
                corrected_in[:half],
                block_inverse[:half],
                preferred_element_type=jnp.float32,
            ),
            jnp.einsum(
                "ekb,ebc->ekc",
                corrected_in[half:],
                block_inverse[half:],
                preferred_element_type=jnp.float32,
            ),
        ],
        axis=0,
    )
    solved = jnp.dot(
        reduced,
        reduced_inverse[0],
        precision=lax.Precision.HIGHEST,
        preferred_element_type=jnp.float32,
    ).astype(jnp.bfloat16)
    correction = jnp.einsum(
        "km,ebm->ekb", solved, interface_basis, preferred_element_type=jnp.float32
    )
    return second + correction


def solution(mesh):
    return jax.shard_map(
        shards,
        mesh=mesh,
        in_specs=(
            P(("dom", "grp"), None, None),
            P(("dom", "grp"), None, None),
            P(("dom", "grp"), None, None),
            P(("dom", "grp"), None),
            P(("dom", "grp")),
            P(("dom", "grp")),
            P(("dom", "grp"), None, None),
            P("dom", None, None),
        ),
        out_specs=P(("dom", "grp"), None, None),
        check_vma=False,
    )
```

```python
import jax
import jax.numpy as jnp
from jax import lax
from jax.sharding import PartitionSpec as P

CAP = 2
LANE = 128


def group_sum(value, axis):
    size = lax.axis_size(axis)
    if size & (size - 1):
        return lax.psum(value, axis)
    bit = 1
    while bit < size:
        pairs = [(i, i ^ bit) for i in range(size)]
        value = value + lax.ppermute(value, axis, pairs)
        bit *= 2
    return value


def shards(
    residual_in,
    block_inverse,
    coupling,
    tile_region,
    tile_source,
    tile_target,
    interface_basis,
    reduced_inverse,
):
    regions = lax.axis_size("dom")
    slots = regions * CAP
    elements = residual_in.shape[0]
    vectors = residual_in.shape[1]
    width = residual_in.shape[2]
    tiles = coupling.shape[0]
    padded = -(-(width + 1) // LANE) * LANE
    initial = jnp.einsum(
        "ekb,ebc->ekc", residual_in, block_inverse, preferred_element_type=jnp.float32
    ).astype(jnp.bfloat16)
    info = lax.optimization_barrier(
        jnp.concatenate([tile_region[:, 0], tile_source, tile_target])
    )
    destination = info[:tiles]
    tile_source = info[tiles : 2 * tiles]
    tile_target = info[2 * tiles :]
    order = jnp.arange(tiles, dtype=jnp.int32)
    same = destination[:, None] == destination[None, :]
    tile_rank = jnp.sum(same & (order[None, :] < order[:, None]), axis=1).astype(jnp.int32)
    slot_index = destination * CAP + tile_rank
    slot_ids = jnp.arange(slots, dtype=jnp.int32)
    hit = slot_index[None, :] == slot_ids[:, None]
    slot_tile = jnp.where(
        jnp.any(hit, axis=1), jnp.sum(jnp.where(hit, order[None, :], 0), axis=1), tiles
    ).astype(jnp.int32)
    sources = initial[tile_source]
    middle = tiles // 2
    local_products = jnp.concatenate(
        [
            jnp.einsum(
                "tkb,tbc->tkc",
                sources[:middle],
                coupling[:middle],
                preferred_element_type=jnp.float32,
            ),
            jnp.einsum(
                "tkb,tbc->tkc",
                sources[middle:],
                coupling[middle:],
                preferred_element_type=jnp.float32,
            ),
        ],
        axis=0,
    ).astype(jnp.bfloat16)
    marks = jnp.concatenate([tile_target, jnp.full((1,), -1, jnp.int32)]).astype(jnp.bfloat16)
    column = lax.broadcasted_iota(jnp.int32, (tiles + 1, vectors, padded - width), 2)
    row = lax.broadcasted_iota(jnp.int32, (tiles + 1, vectors, padded - width), 1)
    tail = jnp.where((column == 0) & (row == 0), marks[:, None, None], jnp.bfloat16(0))
    body = jnp.concatenate(
        [local_products, jnp.zeros((1, vectors, width), jnp.bfloat16)], axis=0
    )
    extended = jnp.concatenate([body, tail], axis=2)
    product_buffer = extended[slot_tile]
    received = lax.all_to_all(
        product_buffer.reshape(regions, CAP, vectors, padded),
        "dom",
        split_axis=0,
        concat_axis=0,
        tiled=True,
    ).reshape(slots, vectors, padded)
    targets = received[:, 0, width].astype(jnp.int32)
    products = received[:, :, :width]
    selector = (targets[None, :] == jnp.arange(elements, dtype=jnp.int32)[:, None]).astype(
        jnp.bfloat16
    )
    coupled = jnp.einsum(
        "es,skc->ekc", selector, products, preferred_element_type=jnp.float32
    )
    corrected_in = (residual_in.astype(jnp.float32) - coupled).astype(jnp.bfloat16)
    projected = jnp.einsum(
        "ebc,ecm->ebm", block_inverse, interface_basis, preferred_element_type=jnp.float32
    )
    partial_reduced = jnp.einsum(
        "ekb,ebm->km",
        corrected_in,
        lax.optimization_barrier(projected.astype(jnp.bfloat16)),
        preferred_element_type=jnp.float32,
    )
    reduced = group_sum(partial_reduced, "grp")
    half = elements // 2
    second = jnp.concatenate(
        [
            jnp.einsum(
                "ekb,ebc->ekc",
                corrected_in[:half],
                block_inverse[:half],
                preferred_element_type=jnp.float32,
            ),
            jnp.einsum(
                "ekb,ebc->ekc",
                corrected_in[half:],
                block_inverse[half:],
                preferred_element_type=jnp.float32,
            ),
        ],
        axis=0,
    )
    solved = jnp.dot(
        reduced,
        reduced_inverse[0],
        precision=lax.Precision.HIGHEST,
        preferred_element_type=jnp.float32,
    ).astype(jnp.bfloat16)
    correction = jnp.einsum(
        "km,ebm->ekb", solved, interface_basis, preferred_element_type=jnp.float32
    )
    return second + correction


def solution(mesh):
    return jax.shard_map(
        shards,
        mesh=mesh,
        in_specs=(
            P(("dom", "grp"), None, None),
            P(("dom", "grp"), None, None),
            P(("dom", "grp"), None, None),
            P(("dom", "grp"), None),
            P(("dom", "grp")),
            P(("dom", "grp")),
            P(("dom", "grp"), None, None),
            P("dom", None, None),
        ),
        out_specs=P(("dom", "grp"), None, None),
        check_vma=False,
    )
```

```python
import jax
import jax.numpy as jnp
from jax import lax
from jax.sharding import PartitionSpec as P

CAP = 2
LANE = 128


def group_sum(value, axis):
    size = lax.axis_size(axis)
    if size & (size - 1):
        return lax.psum(value, axis)
    bit = 1
    while bit < size:
        pairs = [(i, i ^ bit) for i in range(size)]
        value = value + lax.ppermute(value, axis, pairs)
        bit *= 2
    return value


def shards(
    residual_in,
    block_inverse,
    coupling,
    tile_region,
    tile_source,
    tile_target,
    interface_basis,
    reduced_inverse,
):
    regions = lax.axis_size("dom")
    slots = regions * CAP
    elements = residual_in.shape[0]
    vectors = residual_in.shape[1]
    width = residual_in.shape[2]
    tiles = coupling.shape[0]
    padded = -(-(width + 1) // LANE) * LANE
    initial = jnp.einsum(
        "ekb,ebc->ekc", residual_in, block_inverse, preferred_element_type=jnp.float32
    ).astype(jnp.bfloat16)
    info = lax.optimization_barrier(
        jnp.concatenate([tile_region[:, 0], tile_source, tile_target])
    )
    destination = info[:tiles]
    tile_source = info[tiles : 2 * tiles]
    tile_target = info[2 * tiles :]
    order = jnp.arange(tiles, dtype=jnp.int32)
    same = destination[:, None] == destination[None, :]
    tile_rank = jnp.sum(same & (order[None, :] < order[:, None]), axis=1).astype(jnp.int32)
    slot_index = destination * CAP + tile_rank
    slot_ids = jnp.arange(slots, dtype=jnp.int32)
    hit = slot_index[None, :] == slot_ids[:, None]
    slot_tile = jnp.where(
        jnp.any(hit, axis=1), jnp.sum(jnp.where(hit, order[None, :], 0), axis=1), tiles
    ).astype(jnp.int32)
    sources = initial[tile_source]
    cut = min(width, 3 * LANE)
    local_products = (
        jnp.einsum(
            "tkb,tbc->tkc",
            sources[:, :, :cut],
            coupling[:, :cut, :],
            preferred_element_type=jnp.float32,
        )
        + jnp.einsum(
            "tkb,tbc->tkc",
            sources[:, :, cut:],
            coupling[:, cut:, :],
            preferred_element_type=jnp.float32,
        )
    ).astype(jnp.bfloat16)
    marks = jnp.concatenate([tile_target, jnp.full((1,), -1, jnp.int32)]).astype(jnp.bfloat16)
    column = lax.broadcasted_iota(jnp.int32, (tiles + 1, vectors, padded - width), 2)
    row = lax.broadcasted_iota(jnp.int32, (tiles + 1, vectors, padded - width), 1)
    tail = jnp.where((column == 0) & (row == 0), marks[:, None, None], jnp.bfloat16(0))
    body = jnp.concatenate(
        [local_products, jnp.zeros((1, vectors, width), jnp.bfloat16)], axis=0
    )
    extended = jnp.concatenate([body, tail], axis=2)
    product_buffer = extended[slot_tile]
    received = lax.all_to_all(
        product_buffer.reshape(regions, CAP, vectors, padded),
        "dom",
        split_axis=0,
        concat_axis=0,
        tiled=True,
    ).reshape(slots, vectors, padded)
    targets = received[:, 0, width].astype(jnp.int32)
    products = received[:, :, :width]
    selector = (targets[None, :] == jnp.arange(elements, dtype=jnp.int32)[:, None]).astype(
        jnp.bfloat16
    )
    coupled = jnp.einsum(
        "es,skc->ekc", selector, products, preferred_element_type=jnp.float32
    )
    corrected_in = (residual_in.astype(jnp.float32) - coupled).astype(jnp.bfloat16)
    projected = jnp.einsum(
        "ebc,ecm->ebm", block_inverse, interface_basis, preferred_element_type=jnp.float32
    )
    partial_reduced = jnp.einsum(
        "ekb,ebm->km",
        corrected_in,
        lax.optimization_barrier(projected.astype(jnp.bfloat16)),
        preferred_element_type=jnp.float32,
    )
    reduced = group_sum(partial_reduced, "grp")
    half = elements // 2
    second = jnp.concatenate(
        [
            jnp.einsum(
                "ekb,ebc->ekc",
                corrected_in[:half],
                block_inverse[:half],
                preferred_element_type=jnp.float32,
            ),
            jnp.einsum(
                "ekb,ebc->ekc",
                corrected_in[half:],
                block_inverse[half:],
                preferred_element_type=jnp.float32,
            ),
        ],
        axis=0,
    )
    solved = jnp.dot(
        reduced,
        reduced_inverse[0],
        precision=lax.Precision.HIGHEST,
        preferred_element_type=jnp.float32,
    ).astype(jnp.bfloat16)
    correction = jnp.einsum(
        "km,ebm->ekb", solved, interface_basis, preferred_element_type=jnp.float32
    )
    return second + correction


def solution(mesh):
    return jax.shard_map(
        shards,
        mesh=mesh,
        in_specs=(
            P(("dom", "grp"), None, None),
            P(("dom", "grp"), None, None),
            P(("dom", "grp"), None, None),
            P(("dom", "grp"), None),
            P(("dom", "grp")),
            P(("dom", "grp")),
            P(("dom", "grp"), None, None),
            P("dom", None, None),
        ),
        out_specs=P(("dom", "grp"), None, None),
        check_vma=False,
    )
```

```python
import jax
import jax.numpy as jnp
from jax import lax
from jax.experimental.layout import Layout, with_layout_constraint
from jax.sharding import PartitionSpec as P

CAP = 2
LANE = 128


def group_sum(value, axis):
    size = lax.axis_size(axis)
    if size & (size - 1):
        return lax.psum(value, axis)
    bit = 1
    while bit < size:
        pairs = [(i, i ^ bit) for i in range(size)]
        value = value + lax.ppermute(value, axis, pairs)
        bit *= 2
    return value


def shards(
    residual_in,
    block_inverse,
    coupling,
    tile_region,
    tile_source,
    tile_target,
    interface_basis,
    reduced_inverse,
):
    regions = lax.axis_size("dom")
    slots = regions * CAP
    elements = residual_in.shape[0]
    vectors = residual_in.shape[1]
    width = residual_in.shape[2]
    tiles = coupling.shape[0]
    padded = -(-(width + 1) // LANE) * LANE
    initial = jnp.einsum(
        "ekb,ebc->ekc", residual_in, block_inverse, preferred_element_type=jnp.float32
    ).astype(jnp.bfloat16)
    info = lax.optimization_barrier(
        jnp.concatenate([tile_region[:, 0], tile_source, tile_target])
    )
    destination = info[:tiles]
    tile_source = info[tiles : 2 * tiles]
    tile_target = info[2 * tiles :]
    order = jnp.arange(tiles, dtype=jnp.int32)
    same = destination[:, None] == destination[None, :]
    tile_rank = jnp.sum(same & (order[None, :] < order[:, None]), axis=1).astype(jnp.int32)
    slot_index = destination * CAP + tile_rank
    slot_ids = jnp.arange(slots, dtype=jnp.int32)
    hit = slot_index[None, :] == slot_ids[:, None]
    slot_tile = jnp.where(
        jnp.any(hit, axis=1), jnp.sum(jnp.where(hit, order[None, :], 0), axis=1), tiles
    ).astype(jnp.int32)
    sources = initial[tile_source]
    local_products = jnp.einsum(
        "tkb,tbc->tkc", sources, coupling, preferred_element_type=jnp.float32
    ).astype(jnp.bfloat16)
    marks = jnp.concatenate([tile_target, jnp.full((1,), -1, jnp.int32)]).astype(jnp.bfloat16)
    column = lax.broadcasted_iota(jnp.int32, (tiles + 1, vectors, padded - width), 2)
    row = lax.broadcasted_iota(jnp.int32, (tiles + 1, vectors, padded - width), 1)
    tail = jnp.where((column == 0) & (row == 0), marks[:, None, None], jnp.bfloat16(0))
    body = jnp.concatenate(
        [local_products, jnp.zeros((1, vectors, width), jnp.bfloat16)], axis=0
    )
    extended = jnp.concatenate([body, tail], axis=2)
    product_buffer = extended[slot_tile]
    received = lax.all_to_all(
        product_buffer.reshape(regions, CAP, vectors, padded),
        "dom",
        split_axis=0,
        concat_axis=0,
        tiled=True,
    ).reshape(slots, vectors, padded)
    targets = received[:, 0, width].astype(jnp.int32)
    products = received[:, :, :width]
    selector = (targets[None, :] == jnp.arange(elements, dtype=jnp.int32)[:, None]).astype(
        jnp.bfloat16
    )
    coupled = jnp.einsum(
        "es,skc->ekc", selector, products, preferred_element_type=jnp.float32
    )
    corrected_in = (residual_in.astype(jnp.float32) - coupled).astype(jnp.bfloat16)
    late_inverse = with_layout_constraint(block_inverse, Layout((0, 1, 2)))
    projected = jnp.einsum(
        "ebc,ecm->ebm", late_inverse, interface_basis, preferred_element_type=jnp.float32
    )
    partial_reduced = jnp.einsum(
        "ekb,ebm->km",
        corrected_in,
        lax.optimization_barrier(projected.astype(jnp.bfloat16)),
        preferred_element_type=jnp.float32,
    )
    reduced = group_sum(partial_reduced, "grp")
    half = elements // 2
    second = jnp.concatenate(
        [
            jnp.einsum(
                "ekb,ebc->ekc",
                corrected_in[:half],
                late_inverse[:half],
                preferred_element_type=jnp.float32,
            ),
            jnp.einsum(
                "ekb,ebc->ekc",
                corrected_in[half:],
                late_inverse[half:],
                preferred_element_type=jnp.float32,
            ),
        ],
        axis=0,
    )
    solved = jnp.dot(
        reduced,
        reduced_inverse[0],
        precision=lax.Precision.HIGHEST,
        preferred_element_type=jnp.float32,
    ).astype(jnp.bfloat16)
    correction = jnp.einsum(
        "km,ebm->ekb", solved, interface_basis, preferred_element_type=jnp.float32
    )
    return second + correction


def solution(mesh):
    return jax.shard_map(
        shards,
        mesh=mesh,
        in_specs=(
            P(("dom", "grp"), None, None),
            P(("dom", "grp"), None, None),
            P(("dom", "grp"), None, None),
            P(("dom", "grp"), None),
            P(("dom", "grp")),
            P(("dom", "grp")),
            P(("dom", "grp"), None, None),
            P("dom", None, None),
        ),
        out_specs=P(("dom", "grp"), None, None),
        check_vma=False,
    )
```

```python
import jax
import jax.numpy as jnp
from jax import lax
from jax.experimental import pallas as pl
from jax.experimental.pallas import tpu as pltpu
from jax.sharding import PartitionSpec as P

CAP = 2
LANE = 128


def resident(value):
    def kernel(source, target, flag):
        copy = pltpu.make_async_copy(source, target, flag.at[0])
        copy.start()
        copy.wait()

    return pl.pallas_call(
        kernel,
        in_specs=[pl.BlockSpec(memory_space=pl.ANY)],
        out_specs=pl.BlockSpec(memory_space=pltpu.VMEM),
        out_shape=jax.ShapeDtypeStruct(value.shape, value.dtype),
        scratch_shapes=[pltpu.SemaphoreType.DMA((1,))],
        compiler_params=pltpu.CompilerParams(vmem_limit_bytes=48 * 1024 * 1024),
    )(value)


def group_sum(value, axis):
    size = lax.axis_size(axis)
    if size & (size - 1):
        return lax.psum(value, axis)
    bit = 1
    while bit < size:
        pairs = [(i, i ^ bit) for i in range(size)]
        value = value + lax.ppermute(value, axis, pairs)
        bit *= 2
    return value


def shards(
    residual_in,
    block_inverse,
    coupling,
    tile_region,
    tile_source,
    tile_target,
    interface_basis,
    reduced_inverse,
):
    regions = lax.axis_size("dom")
    slots = regions * CAP
    elements = residual_in.shape[0]
    vectors = residual_in.shape[1]
    width = residual_in.shape[2]
    tiles = coupling.shape[0]
    padded = -(-(width + 1) // LANE) * LANE
    initial = jnp.einsum(
        "ekb,ebc->ekc", residual_in, block_inverse, preferred_element_type=jnp.float32
    ).astype(jnp.bfloat16)
    info = lax.optimization_barrier(
        jnp.concatenate([tile_region[:, 0], tile_source, tile_target])
    )
    destination = info[:tiles]
    tile_source = info[tiles : 2 * tiles]
    tile_target = info[2 * tiles :]
    order = jnp.arange(tiles, dtype=jnp.int32)
    same = destination[:, None] == destination[None, :]
    tile_rank = jnp.sum(same & (order[None, :] < order[:, None]), axis=1).astype(jnp.int32)
    slot_index = destination * CAP + tile_rank
    slot_ids = jnp.arange(slots, dtype=jnp.int32)
    hit = slot_index[None, :] == slot_ids[:, None]
    slot_tile = jnp.where(
        jnp.any(hit, axis=1), jnp.sum(jnp.where(hit, order[None, :], 0), axis=1), tiles
    ).astype(jnp.int32)
    sources = initial[tile_source]
    local_products = jnp.einsum(
        "tkb,tbc->tkc", sources, coupling, preferred_element_type=jnp.float32
    ).astype(jnp.bfloat16)
    marks = jnp.concatenate([tile_target, jnp.full((1,), -1, jnp.int32)]).astype(jnp.bfloat16)
    column = lax.broadcasted_iota(jnp.int32, (tiles + 1, vectors, padded - width), 2)
    row = lax.broadcasted_iota(jnp.int32, (tiles + 1, vectors, padded - width), 1)
    tail = jnp.where((column == 0) & (row == 0), marks[:, None, None], jnp.bfloat16(0))
    body = jnp.concatenate(
        [local_products, jnp.zeros((1, vectors, width), jnp.bfloat16)], axis=0
    )
    extended = jnp.concatenate([body, tail], axis=2)
    product_buffer = extended[slot_tile]
    received = lax.all_to_all(
        product_buffer.reshape(regions, CAP, vectors, padded),
        "dom",
        split_axis=0,
        concat_axis=0,
        tiled=True,
    ).reshape(slots, vectors, padded)
    targets = received[:, 0, width].astype(jnp.int32)
    products = received[:, :, :width]
    selector = (targets[None, :] == jnp.arange(elements, dtype=jnp.int32)[:, None]).astype(
        jnp.bfloat16
    )
    coupled = jnp.einsum(
        "es,skc->ekc", selector, products, preferred_element_type=jnp.float32
    )
    corrected_in = (residual_in.astype(jnp.float32) - coupled).astype(jnp.bfloat16)
    late_inverse = jnp.transpose(resident(jnp.transpose(block_inverse, (1, 0, 2))), (1, 0, 2))
    projected = jnp.einsum(
        "ebc,ecm->ebm", late_inverse, interface_basis, preferred_element_type=jnp.float32
    )
    partial_reduced = jnp.einsum(
        "ekb,ebm->km",
        corrected_in,
        lax.optimization_barrier(projected.astype(jnp.bfloat16)),
        preferred_element_type=jnp.float32,
    )
    reduced = group_sum(partial_reduced, "grp")
    half = elements // 2
    second = jnp.concatenate(
        [
            jnp.einsum(
                "ekb,ebc->ekc",
                corrected_in[:half],
                late_inverse[:half],
                preferred_element_type=jnp.float32,
            ),
            jnp.einsum(
                "ekb,ebc->ekc",
                corrected_in[half:],
                late_inverse[half:],
                preferred_element_type=jnp.float32,
            ),
        ],
        axis=0,
    )
    solved = jnp.dot(
        reduced,
        reduced_inverse[0],
        precision=lax.Precision.HIGHEST,
        preferred_element_type=jnp.float32,
    ).astype(jnp.bfloat16)
    correction = jnp.einsum(
        "km,ebm->ekb", solved, interface_basis, preferred_element_type=jnp.float32
    )
    return second + correction


def solution(mesh):
    return jax.shard_map(
        shards,
        mesh=mesh,
        in_specs=(
            P(("dom", "grp"), None, None),
            P(("dom", "grp"), None, None),
            P(("dom", "grp"), None, None),
            P(("dom", "grp"), None),
            P(("dom", "grp")),
            P(("dom", "grp")),
            P(("dom", "grp"), None, None),
            P("dom", None, None),
        ),
        out_specs=P(("dom", "grp"), None, None),
        check_vma=False,
    )
```

```python
import jax
import jax.numpy as jnp
from jax import lax
from jax.experimental import pallas as pl
from jax.experimental.pallas import tpu as pltpu
from jax.sharding import PartitionSpec as P

CAP = 2
LANE = 128


def resident(value):
    parts = 5
    rows = value.shape[0]
    edges = [rows * i // parts for i in range(parts + 1)]

    def kernel(source, target, flag):
        copies = [
            pltpu.make_async_copy(
                source.at[pl.ds(lo, hi - lo)], target.at[pl.ds(lo, hi - lo)], flag.at[i]
            )
            for i, (lo, hi) in enumerate(zip(edges[:-1], edges[1:]))
        ]
        for copy in copies:
            copy.start()
        for copy in copies:
            copy.wait()

    return pl.pallas_call(
        kernel,
        in_specs=[pl.BlockSpec(memory_space=pl.ANY)],
        out_specs=pl.BlockSpec(memory_space=pltpu.VMEM),
        out_shape=jax.ShapeDtypeStruct(value.shape, value.dtype),
        scratch_shapes=[pltpu.SemaphoreType.DMA((parts,))],
        compiler_params=pltpu.CompilerParams(vmem_limit_bytes=48 * 1024 * 1024),
    )(value)


def group_sum(value, axis):
    size = lax.axis_size(axis)
    if size & (size - 1):
        return lax.psum(value, axis)
    bit = 1
    while bit < size:
        pairs = [(i, i ^ bit) for i in range(size)]
        value = value + lax.ppermute(value, axis, pairs)
        bit *= 2
    return value


def shards(
    residual_in,
    block_inverse,
    coupling,
    tile_region,
    tile_source,
    tile_target,
    interface_basis,
    reduced_inverse,
):
    regions = lax.axis_size("dom")
    slots = regions * CAP
    elements = residual_in.shape[0]
    vectors = residual_in.shape[1]
    width = residual_in.shape[2]
    tiles = coupling.shape[0]
    padded = -(-(width + 1) // LANE) * LANE
    initial = jnp.einsum(
        "ekb,ebc->ekc", residual_in, block_inverse, preferred_element_type=jnp.float32
    ).astype(jnp.bfloat16)
    info = lax.optimization_barrier(
        jnp.concatenate([tile_region[:, 0], tile_source, tile_target])
    )
    destination = info[:tiles]
    tile_source = info[tiles : 2 * tiles]
    tile_target = info[2 * tiles :]
    order = jnp.arange(tiles, dtype=jnp.int32)
    same = destination[:, None] == destination[None, :]
    tile_rank = jnp.sum(same & (order[None, :] < order[:, None]), axis=1).astype(jnp.int32)
    slot_index = destination * CAP + tile_rank
    slot_ids = jnp.arange(slots, dtype=jnp.int32)
    hit = slot_index[None, :] == slot_ids[:, None]
    slot_tile = jnp.where(
        jnp.any(hit, axis=1), jnp.sum(jnp.where(hit, order[None, :], 0), axis=1), tiles
    ).astype(jnp.int32)
    sources = initial[tile_source]
    local_products = jnp.einsum(
        "tkb,tbc->tkc",
        sources,
        jnp.transpose(resident(jnp.transpose(coupling, (1, 0, 2))), (1, 0, 2)),
        preferred_element_type=jnp.float32,
    ).astype(jnp.bfloat16)
    marks = jnp.concatenate([tile_target, jnp.full((1,), -1, jnp.int32)]).astype(jnp.bfloat16)
    column = lax.broadcasted_iota(jnp.int32, (tiles + 1, vectors, padded - width), 2)
    row = lax.broadcasted_iota(jnp.int32, (tiles + 1, vectors, padded - width), 1)
    tail = jnp.where((column == 0) & (row == 0), marks[:, None, None], jnp.bfloat16(0))
    body = jnp.concatenate(
        [local_products, jnp.zeros((1, vectors, width), jnp.bfloat16)], axis=0
    )
    extended = jnp.concatenate([body, tail], axis=2)
    product_buffer = extended[slot_tile]
    received = lax.all_to_all(
        product_buffer.reshape(regions, CAP, vectors, padded),
        "dom",
        split_axis=0,
        concat_axis=0,
        tiled=True,
    ).reshape(slots, vectors, padded)
    targets = received[:, 0, width].astype(jnp.int32)
    products = received[:, :, :width]
    selector = (targets[None, :] == jnp.arange(elements, dtype=jnp.int32)[:, None]).astype(
        jnp.bfloat16
    )
    coupled = jnp.einsum(
        "es,skc->ekc", selector, products, preferred_element_type=jnp.float32
    )
    corrected_in = (residual_in.astype(jnp.float32) - coupled).astype(jnp.bfloat16)
    late_inverse = jnp.transpose(resident(jnp.transpose(block_inverse, (1, 0, 2))), (1, 0, 2))
    projected = jnp.einsum(
        "ebc,ecm->ebm", late_inverse, interface_basis, preferred_element_type=jnp.float32
    )
    partial_reduced = jnp.einsum(
        "ekb,ebm->km",
        corrected_in,
        lax.optimization_barrier(projected.astype(jnp.bfloat16)),
        preferred_element_type=jnp.float32,
    )
    reduced = group_sum(partial_reduced, "grp")
    half = elements // 2
    second = jnp.concatenate(
        [
            jnp.einsum(
                "ekb,ebc->ekc",
                corrected_in[:half],
                late_inverse[:half],
                preferred_element_type=jnp.float32,
            ),
            jnp.einsum(
                "ekb,ebc->ekc",
                corrected_in[half:],
                late_inverse[half:],
                preferred_element_type=jnp.float32,
            ),
        ],
        axis=0,
    )
    solved = jnp.dot(
        reduced,
        reduced_inverse[0],
        precision=lax.Precision.HIGHEST,
        preferred_element_type=jnp.float32,
    ).astype(jnp.bfloat16)
    correction = jnp.einsum(
        "km,ebm->ekb", solved, interface_basis, preferred_element_type=jnp.float32
    )
    return second + correction


def solution(mesh):
    return jax.shard_map(
        shards,
        mesh=mesh,
        in_specs=(
            P(("dom", "grp"), None, None),
            P(("dom", "grp"), None, None),
            P(("dom", "grp"), None, None),
            P(("dom", "grp"), None),
            P(("dom", "grp")),
            P(("dom", "grp")),
            P(("dom", "grp"), None, None),
            P("dom", None, None),
        ),
        out_specs=P(("dom", "grp"), None, None),
        check_vma=False,
    )
```

```python
import jax
import jax.numpy as jnp
from jax import lax
from jax.experimental import pallas as pl
from jax.experimental.pallas import tpu as pltpu
from jax.sharding import PartitionSpec as P

CAP = 2
LANE = 128


def resident(value):
    def kernel(source, target, flag):
        copy = pltpu.make_async_copy(source, target, flag.at[0])
        copy.start()
        copy.wait()

    return pl.pallas_call(
        kernel,
        in_specs=[pl.BlockSpec(memory_space=pl.ANY)],
        out_specs=pl.BlockSpec(memory_space=pltpu.VMEM),
        out_shape=jax.ShapeDtypeStruct(value.shape, value.dtype),
        scratch_shapes=[pltpu.SemaphoreType.DMA((1,))],
        compiler_params=pltpu.CompilerParams(vmem_limit_bytes=48 * 1024 * 1024),
    )(value)


def group_sum(value, axis):
    size = lax.axis_size(axis)
    if size & (size - 1):
        return lax.psum(value, axis)
    if size == 8:
        ring = size // 2
        value = value + lax.ppermute(value, axis, [(i, i ^ 1) for i in range(size)])
        left = lax.ppermute(value, axis, [(i, (i + 2) % size) for i in range(size)])
        right = lax.ppermute(value, axis, [(i, (i - 2) % size) for i in range(size)])
        far = lax.ppermute(right, axis, [(i, (i - 2) % size) for i in range(size)])
        stacked = jnp.stack([value, right, far, left])
        place = lax.axis_index(axis) // 2
        parts = [stacked[(k - place) % ring] for k in range(ring)]
        return (parts[0] + parts[1]) + (parts[2] + parts[3])
    bit = 1
    while bit < size:
        pairs = [(i, i ^ bit) for i in range(size)]
        value = value + lax.ppermute(value, axis, pairs)
        bit *= 2
    return value


def shards(
    residual_in,
    block_inverse,
    coupling,
    tile_region,
    tile_source,
    tile_target,
    interface_basis,
    reduced_inverse,
):
    regions = lax.axis_size("dom")
    slots = regions * CAP
    elements = residual_in.shape[0]
    vectors = residual_in.shape[1]
    width = residual_in.shape[2]
    tiles = coupling.shape[0]
    padded = -(-(width + 1) // LANE) * LANE
    initial = jnp.einsum(
        "ekb,ebc->ekc", residual_in, block_inverse, preferred_element_type=jnp.float32
    ).astype(jnp.bfloat16)
    info = lax.optimization_barrier(
        jnp.concatenate([tile_region[:, 0], tile_source, tile_target])
    )
    destination = info[:tiles]
    tile_source = info[tiles : 2 * tiles]
    tile_target = info[2 * tiles :]
    order = jnp.arange(tiles, dtype=jnp.int32)
    same = destination[:, None] == destination[None, :]
    tile_rank = jnp.sum(same & (order[None, :] < order[:, None]), axis=1).astype(jnp.int32)
    slot_index = destination * CAP + tile_rank
    slot_ids = jnp.arange(slots, dtype=jnp.int32)
    hit = slot_index[None, :] == slot_ids[:, None]
    slot_tile = jnp.where(
        jnp.any(hit, axis=1), jnp.sum(jnp.where(hit, order[None, :], 0), axis=1), tiles
    ).astype(jnp.int32)
    sources = initial[tile_source]
    local_products = jnp.einsum(
        "tkb,tbc->tkc", sources, coupling, preferred_element_type=jnp.float32
    ).astype(jnp.bfloat16)
    marks = jnp.concatenate([tile_target, jnp.full((1,), -1, jnp.int32)]).astype(jnp.bfloat16)
    column = lax.broadcasted_iota(jnp.int32, (tiles + 1, vectors, padded - width), 2)
    row = lax.broadcasted_iota(jnp.int32, (tiles + 1, vectors, padded - width), 1)
    tail = jnp.where((column == 0) & (row == 0), marks[:, None, None], jnp.bfloat16(0))
    body = jnp.concatenate(
        [local_products, jnp.zeros((1, vectors, width), jnp.bfloat16)], axis=0
    )
    extended = jnp.concatenate([body, tail], axis=2)
    product_buffer = extended[slot_tile]
    received = lax.all_to_all(
        product_buffer.reshape(regions, CAP, vectors, padded),
        "dom",
        split_axis=0,
        concat_axis=0,
        tiled=True,
    ).reshape(slots, vectors, padded)
    targets = received[:, 0, width].astype(jnp.int32)
    products = received[:, :, :width]
    selector = (targets[None, :] == jnp.arange(elements, dtype=jnp.int32)[:, None]).astype(
        jnp.bfloat16
    )
    coupled = jnp.einsum(
        "es,skc->ekc", selector, products, preferred_element_type=jnp.float32
    )
    corrected_in = (residual_in.astype(jnp.float32) - coupled).astype(jnp.bfloat16)
    late_inverse = jnp.transpose(resident(jnp.transpose(block_inverse, (1, 0, 2))), (1, 0, 2))
    projected = jnp.einsum(
        "ebc,ecm->ebm", late_inverse, interface_basis, preferred_element_type=jnp.float32
    )
    partial_reduced = jnp.einsum(
        "ekb,ebm->km",
        corrected_in,
        lax.optimization_barrier(projected.astype(jnp.bfloat16)),
        preferred_element_type=jnp.float32,
    )
    reduced = group_sum(partial_reduced, "grp")
    half = elements // 2
    second = jnp.concatenate(
        [
            jnp.einsum(
                "ekb,ebc->ekc",
                corrected_in[:half],
                late_inverse[:half],
                preferred_element_type=jnp.float32,
            ),
            jnp.einsum(
                "ekb,ebc->ekc",
                corrected_in[half:],
                late_inverse[half:],
                preferred_element_type=jnp.float32,
            ),
        ],
        axis=0,
    )
    solved = jnp.dot(
        reduced,
        reduced_inverse[0],
        precision=lax.Precision.HIGHEST,
        preferred_element_type=jnp.float32,
    ).astype(jnp.bfloat16)
    correction = jnp.einsum(
        "km,ebm->ekb", solved, interface_basis, preferred_element_type=jnp.float32
    )
    return second + correction


def solution(mesh):
    return jax.shard_map(
        shards,
        mesh=mesh,
        in_specs=(
            P(("dom", "grp"), None, None),
            P(("dom", "grp"), None, None),
            P(("dom", "grp"), None, None),
            P(("dom", "grp"), None),
            P(("dom", "grp")),
            P(("dom", "grp")),
            P(("dom", "grp"), None, None),
            P("dom", None, None),
        ),
        out_specs=P(("dom", "grp"), None, None),
        check_vma=False,
    )
```

```python
import jax
import jax.numpy as jnp
from jax import lax
from jax.experimental import pallas as pl
from jax.experimental.pallas import tpu as pltpu
from jax.sharding import PartitionSpec as P

CAP = 2
LANE = 128


def resident(value):
    def kernel(source, target, flag):
        copy = pltpu.make_async_copy(source, target, flag.at[0])
        copy.start()
        copy.wait()

    return pl.pallas_call(
        kernel,
        in_specs=[pl.BlockSpec(memory_space=pl.ANY)],
        out_specs=pl.BlockSpec(memory_space=pltpu.VMEM),
        out_shape=jax.ShapeDtypeStruct(value.shape, value.dtype),
        scratch_shapes=[pltpu.SemaphoreType.DMA((1,))],
        compiler_params=pltpu.CompilerParams(vmem_limit_bytes=48 * 1024 * 1024),
    )(value)


def group_sum(value, axis):
    size = lax.axis_size(axis)
    if size & (size - 1):
        return lax.psum(value, axis)
    bit = 1
    while bit < size:
        pairs = [(i, i ^ bit) for i in range(size)]
        value = value + lax.ppermute(value, axis, pairs)
        bit *= 2
    return value


def shards(
    residual_in,
    block_inverse,
    coupling,
    tile_region,
    tile_source,
    tile_target,
    interface_basis,
    reduced_inverse,
):
    regions = lax.axis_size("dom")
    slots = regions * CAP
    elements = residual_in.shape[0]
    vectors = residual_in.shape[1]
    width = residual_in.shape[2]
    tiles = coupling.shape[0]
    padded = -(-(width + 1) // LANE) * LANE
    initial = jnp.einsum(
        "ekb,ebc->ekc", residual_in, block_inverse, preferred_element_type=jnp.float32
    ).astype(jnp.bfloat16)
    info = lax.optimization_barrier(
        jnp.concatenate([tile_region[:, 0], tile_source, tile_target])
    )
    destination = info[:tiles]
    tile_source = info[tiles : 2 * tiles]
    tile_target = info[2 * tiles :]
    order = jnp.arange(tiles, dtype=jnp.int32)
    same = destination[:, None] == destination[None, :]
    tile_rank = jnp.sum(same & (order[None, :] < order[:, None]), axis=1).astype(jnp.int32)
    slot_index = destination * CAP + tile_rank
    slot_ids = jnp.arange(slots, dtype=jnp.int32)
    hit = slot_index[None, :] == slot_ids[:, None]
    slot_tile = jnp.where(
        jnp.any(hit, axis=1), jnp.sum(jnp.where(hit, order[None, :], 0), axis=1), tiles
    ).astype(jnp.int32)
    picks = (tile_source[:, None] == jnp.arange(elements, dtype=jnp.int32)[None, :]).astype(
        jnp.bfloat16
    )
    sources = jnp.einsum(
        "te,ekb->tkb", picks, initial, preferred_element_type=jnp.float32
    ).astype(jnp.bfloat16)
    local_products = jnp.einsum(
        "tkb,tbc->tkc", sources, coupling, preferred_element_type=jnp.float32
    ).astype(jnp.bfloat16)
    marks = jnp.concatenate([tile_target, jnp.full((1,), -1, jnp.int32)]).astype(jnp.bfloat16)
    column = lax.broadcasted_iota(jnp.int32, (tiles + 1, vectors, padded - width), 2)
    row = lax.broadcasted_iota(jnp.int32, (tiles + 1, vectors, padded - width), 1)
    tail = jnp.where((column == 0) & (row == 0), marks[:, None, None], jnp.bfloat16(0))
    body = jnp.concatenate(
        [local_products, jnp.zeros((1, vectors, width), jnp.bfloat16)], axis=0
    )
    extended = jnp.concatenate([body, tail], axis=2)
    product_buffer = extended[slot_tile]
    received = lax.all_to_all(
        product_buffer.reshape(regions, CAP, vectors, padded),
        "dom",
        split_axis=0,
        concat_axis=0,
        tiled=True,
    ).reshape(slots, vectors, padded)
    targets = received[:, 0, width].astype(jnp.int32)
    products = received[:, :, :width]
    selector = (targets[None, :] == jnp.arange(elements, dtype=jnp.int32)[:, None]).astype(
        jnp.bfloat16
    )
    coupled = jnp.einsum(
        "es,skc->ekc", selector, products, preferred_element_type=jnp.float32
    )
    corrected_in = (residual_in.astype(jnp.float32) - coupled).astype(jnp.bfloat16)
    late_inverse = jnp.transpose(resident(jnp.transpose(block_inverse, (1, 0, 2))), (1, 0, 2))
    projected = jnp.einsum(
        "ebc,ecm->ebm", late_inverse, interface_basis, preferred_element_type=jnp.float32
    )
    partial_reduced = jnp.einsum(
        "ekb,ebm->km",
        corrected_in,
        lax.optimization_barrier(projected.astype(jnp.bfloat16)),
        preferred_element_type=jnp.float32,
    )
    reduced = group_sum(partial_reduced, "grp")
    half = elements // 2
    second = jnp.concatenate(
        [
            jnp.einsum(
                "ekb,ebc->ekc",
                corrected_in[:half],
                late_inverse[:half],
                preferred_element_type=jnp.float32,
            ),
            jnp.einsum(
                "ekb,ebc->ekc",
                corrected_in[half:],
                late_inverse[half:],
                preferred_element_type=jnp.float32,
            ),
        ],
        axis=0,
    )
    solved = jnp.dot(
        reduced,
        reduced_inverse[0],
        precision=lax.Precision.HIGHEST,
        preferred_element_type=jnp.float32,
    ).astype(jnp.bfloat16)
    correction = jnp.einsum(
        "km,ebm->ekb", solved, interface_basis, preferred_element_type=jnp.float32
    )
    return second + correction


def solution(mesh):
    return jax.shard_map(
        shards,
        mesh=mesh,
        in_specs=(
            P(("dom", "grp"), None, None),
            P(("dom", "grp"), None, None),
            P(("dom", "grp"), None, None),
            P(("dom", "grp"), None),
            P(("dom", "grp")),
            P(("dom", "grp")),
            P(("dom", "grp"), None, None),
            P("dom", None, None),
        ),
        out_specs=P(("dom", "grp"), None, None),
        check_vma=False,
    )
```

```python
import jax
import jax.numpy as jnp
from jax import lax
from jax.experimental import pallas as pl
from jax.experimental.pallas import tpu as pltpu
from jax.sharding import PartitionSpec as P

CAP = 2
LANE = 128


def resident(value):
    def kernel(source, target, flag):
        copy = pltpu.make_async_copy(source, target, flag.at[0])
        copy.start()
        copy.wait()

    return pl.pallas_call(
        kernel,
        in_specs=[pl.BlockSpec(memory_space=pl.ANY)],
        out_specs=pl.BlockSpec(memory_space=pltpu.VMEM),
        out_shape=jax.ShapeDtypeStruct(value.shape, value.dtype),
        scratch_shapes=[pltpu.SemaphoreType.DMA((1,))],
        compiler_params=pltpu.CompilerParams(vmem_limit_bytes=48 * 1024 * 1024),
    )(value)


def group_sum(value, axis):
    size = lax.axis_size(axis)
    if size & (size - 1):
        return lax.psum(value, axis)
    bit = 1
    while bit < size:
        pairs = [(i, i ^ bit) for i in range(size)]
        value = value + lax.ppermute(value, axis, pairs)
        bit *= 2
    return value


def shards(
    residual_in,
    block_inverse,
    coupling,
    tile_region,
    tile_source,
    tile_target,
    interface_basis,
    reduced_inverse,
):
    regions = lax.axis_size("dom")
    slots = regions * CAP
    elements = residual_in.shape[0]
    vectors = residual_in.shape[1]
    width = residual_in.shape[2]
    tiles = coupling.shape[0]
    padded = -(-(width + 1) // LANE) * LANE
    initial = jnp.einsum(
        "ekb,ebc->ekc", residual_in, block_inverse, preferred_element_type=jnp.float32
    ).astype(jnp.bfloat16)
    info = lax.optimization_barrier(
        jnp.concatenate([tile_region[:, 0], tile_source, tile_target])
    )
    destination = info[:tiles]
    tile_source = info[tiles : 2 * tiles]
    tile_target = info[2 * tiles :]
    order = jnp.arange(tiles, dtype=jnp.int32)
    same = destination[:, None] == destination[None, :]
    tile_rank = jnp.sum(same & (order[None, :] < order[:, None]), axis=1).astype(jnp.int32)
    slot_index = destination * CAP + tile_rank
    slot_ids = jnp.arange(slots, dtype=jnp.int32)
    hit = slot_index[None, :] == slot_ids[:, None]
    slot_tile = jnp.where(
        jnp.any(hit, axis=1), jnp.sum(jnp.where(hit, order[None, :], 0), axis=1), tiles
    ).astype(jnp.int32)
    picks = (tile_source[:, None] == jnp.arange(elements, dtype=jnp.int32)[None, :]).astype(
        jnp.bfloat16
    )
    sources = jnp.einsum(
        "te,ekb->tkb", picks, initial, preferred_element_type=jnp.float32
    ).astype(jnp.bfloat16)
    local_products = jnp.einsum(
        "tkb,tbc->tkc", sources, coupling, preferred_element_type=jnp.float32
    ).astype(jnp.bfloat16)
    marks = jnp.concatenate([tile_target, jnp.full((1,), -1, jnp.int32)]).astype(jnp.bfloat16)
    column = lax.broadcasted_iota(jnp.int32, (tiles + 1, vectors, padded - width), 2)
    row = lax.broadcasted_iota(jnp.int32, (tiles + 1, vectors, padded - width), 1)
    tail = jnp.where((column == 0) & (row == 0), marks[:, None, None], jnp.bfloat16(0))
    body = jnp.concatenate(
        [local_products, jnp.zeros((1, vectors, width), jnp.bfloat16)], axis=0
    )
    extended = jnp.concatenate([body, tail], axis=2)
    slot_picks = (
        slot_tile[:, None] == jnp.arange(tiles + 1, dtype=jnp.int32)[None, :]
    ).astype(jnp.bfloat16)
    product_buffer = jnp.einsum(
        "st,tkc->skc", slot_picks, extended, preferred_element_type=jnp.float32
    ).astype(jnp.bfloat16)
    received = lax.all_to_all(
        product_buffer.reshape(regions, CAP, vectors, padded),
        "dom",
        split_axis=0,
        concat_axis=0,
        tiled=True,
    ).reshape(slots, vectors, padded)
    targets = received[:, 0, width].astype(jnp.int32)
    products = received[:, :, :width]
    selector = (targets[None, :] == jnp.arange(elements, dtype=jnp.int32)[:, None]).astype(
        jnp.bfloat16
    )
    coupled = jnp.einsum(
        "es,skc->ekc", selector, products, preferred_element_type=jnp.float32
    )
    corrected_in = (residual_in.astype(jnp.float32) - coupled).astype(jnp.bfloat16)
    late_inverse = jnp.transpose(resident(jnp.transpose(block_inverse, (1, 0, 2))), (1, 0, 2))
    projected = jnp.einsum(
        "ebc,ecm->ebm", late_inverse, interface_basis, preferred_element_type=jnp.float32
    )
    partial_reduced = jnp.einsum(
        "ekb,ebm->km",
        corrected_in,
        lax.optimization_barrier(projected.astype(jnp.bfloat16)),
        preferred_element_type=jnp.float32,
    )
    reduced = group_sum(partial_reduced, "grp")
    half = elements // 2
    second = jnp.concatenate(
        [
            jnp.einsum(
                "ekb,ebc->ekc",
                corrected_in[:half],
                late_inverse[:half],
                preferred_element_type=jnp.float32,
            ),
            jnp.einsum(
                "ekb,ebc->ekc",
                corrected_in[half:],
                late_inverse[half:],
                preferred_element_type=jnp.float32,
            ),
        ],
        axis=0,
    )
    solved = jnp.dot(
        reduced,
        reduced_inverse[0],
        precision=lax.Precision.HIGHEST,
        preferred_element_type=jnp.float32,
    ).astype(jnp.bfloat16)
    correction = jnp.einsum(
        "km,ebm->ekb", solved, interface_basis, preferred_element_type=jnp.float32
    )
    return second + correction


def solution(mesh):
    return jax.shard_map(
        shards,
        mesh=mesh,
        in_specs=(
            P(("dom", "grp"), None, None),
            P(("dom", "grp"), None, None),
            P(("dom", "grp"), None, None),
            P(("dom", "grp"), None),
            P(("dom", "grp")),
            P(("dom", "grp")),
            P(("dom", "grp"), None, None),
            P("dom", None, None),
        ),
        out_specs=P(("dom", "grp"), None, None),
        check_vma=False,
    )
```
